512 devices in a mesh: pair: 32 (over z_lo, y), loop: 16 (over x, z_hi, core).
Axes of the slice: x: 4, y: 4, z: 16 (z_hi: 2, z_lo: 8; z = z_hi * 8 + z_lo), core: 2. Of those that a mesh axis runs over, the one named last changes fastest.
Arguments:
- amplitudes: float32 [8192, 8192], P('pair', 'loop'), may hold values from -6 to 6
- integrals: float32 [2048, 8192], P(None, 'loop'), may hold values from -0.0625 to 0.0625
- pair_partner: int32 [8192], P('pair'), may hold values from 0 to 8191, as said below
- virtual_swap: int32 [2048], P('loop'), may hold values from 0 to 2047, as said below
Outputs:
- ladder_sym: float32 [2048, 8192], P('loop', 'pair')
The draws below stay inside these ranges and needn't reach their ends.
Inputs may be any that keep to these rules, and one draw needn't show every extreme that they name: pair_partner[pair_partner[p]] = p, and pair_partner[p] lies in the aligned block of 256 pairs that starts 8192 / 2 pairs further on, counted modulo 8192. virtual_swap[virtual_swap[k]] = k, virtual_swap[k] != k, and virtual_swap[k] lies in the same aligned block of 64 ab pairs as k.
All inputs are finite; a program needn't handle non-finite values.
Results may differ from the reference program's by a relative error of at most 0.000071.
Values sent between devices are 32-bit elements; how exact they have to be, the bound alone decides.
No kernel may reach another device: no remote copies, remote signals or barrier semaphores. Data moves between devices by JAX's collectives and lax.ppermute only.
A program may use at most 64 MiB of HBM per device.

```python
import jax
import jax.numpy as jnp
from jax import lax

AB = 2048
PERM_BLOCK = 64
IJ_DEV = 256
PAIRS = 8192
CD = 8192


def draw_pair_partner(key, part):
    groups = PAIRS // (2 * IJ_DEV)
    keys = jax.random.split(jax.random.fold_in(key, 11), groups)
    perms = jax.vmap(lambda k: jax.random.permutation(k, IJ_DEV))(keys).astype(jnp.int32)
    inverse = jnp.argsort(perms, axis=1, stable=True).astype(jnp.int32)
    offsets = (jnp.arange(groups, dtype=jnp.int32) * IJ_DEV)[:, None]
    lower = perms + offsets + PAIRS // 2
    upper = inverse + offsets
    return jnp.concatenate([lower.reshape(-1), upper.reshape(-1)]).astype(jnp.int32)


def one_block(key):
    order = jax.random.permutation(key, PERM_BLOCK).astype(jnp.int32)
    firsts = order[0::2]
    seconds = order[1::2]
    result = jnp.zeros((PERM_BLOCK,), jnp.int32)
    result = result.at[firsts].set(seconds)
    result = result.at[seconds].set(firsts)
    return result


def draw_virtual_swap(key, part):
    blocks = AB // PERM_BLOCK
    keys = jax.random.split(jax.random.fold_in(key, 23), blocks)
    local = jax.vmap(one_block)(keys)
    offsets = (jnp.arange(blocks, dtype=jnp.int32) * PERM_BLOCK)[:, None]
    return (local + offsets).reshape(-1).astype(jnp.int32)


def block_levels(rng, extent, shards, low, high):
    gain = 1.0
    for dim, shards_of in shards:
        draws = jax.random.uniform(jax.random.fold_in(jax.random.fold_in(rng, 6), dim), (shards_of,), jnp.float32, low / len(shards), high / len(shards))
        gain = gain * jnp.repeat(jnp.exp(draws), extent[dim] // shards_of).reshape((-1,) + (1,) * (len(extent) - 1 - dim))
    return gain


def noise(key, extent, deviation, bound, cuts=(), kind=jnp.bfloat16):
    level = block_levels(key, extent, cuts, -0.22, 0.18) if cuts else 1.0
    drawn = jax.random.normal(key, extent, jnp.float32) * deviation * level
    return jnp.minimum(jnp.maximum(drawn, -bound), bound).astype(kind)


def setup_inputs(seed: int = 0) -> dict:
    arg_keys = jax.random.split(jax.random.key(seed), 5)
    amplitudes = noise(arg_keys[0], (PAIRS, CD), 1.0, 6.0, ((0, 32), (1, 16)), jnp.float32)
    integrals = noise(arg_keys[1], (AB, CD), CD ** -0.5, 0.0625, ((1, 16),), jnp.float32)
    pair_partner = draw_pair_partner(jax.random.fold_in(arg_keys[4], 71), 0)
    virtual_swap = draw_virtual_swap(jax.random.fold_in(arg_keys[4], 71), 0)
    return {"amplitudes": amplitudes, "integrals": integrals, "pair_partner": pair_partner, "virtual_swap": virtual_swap}


def reference(amplitudes, integrals, pair_partner, virtual_swap):
    ladder = lax.dot_general(amplitudes, integrals, (((1,), (1,)), ((), ())), precision=lax.Precision.HIGHEST, preferred_element_type=jnp.float32)
    mirror = jnp.take(jnp.take(ladder, pair_partner, axis=0), virtual_swap, axis=1)
    return (ladder + mirror).T
```

```python
import jax
import jax.numpy as jnp
from jax import lax
from jax.sharding import PartitionSpec as P


def shifted(x, axis, by):
    count = lax.axis_size(axis)
    return lax.ppermute(x, axis, [(i, (i + by) % count) for i in range(count)])


def local(amplitudes, integrals, pair_partner, virtual_swap):
    loop_count = lax.axis_size("loop")
    pair_count = lax.axis_size("pair")
    ab_local = integrals.shape[0] // loop_count
    ij_local = amplitudes.shape[0]
    partial = lax.dot_general(
        integrals,
        amplitudes,
        (((1,), (1,)), ((), ())),
        precision=lax.Precision.HIGHEST,
        preferred_element_type=jnp.float32,
    )
    ladder = lax.psum_scatter(partial, "loop", scatter_dimension=0, tiled=True)
    mirror = shifted(ladder, "pair", pair_count // 2)
    swap_local = virtual_swap - lax.axis_index("loop") * ab_local
    partner_local = pair_partner % ij_local
    mirror = jnp.take(jnp.take(mirror, swap_local, axis=0), partner_local, axis=1)
    return ladder + mirror


def solution(mesh):
    in_specs = (P("pair", "loop"), P(None, "loop"), P("pair"), P("loop"))
    out_specs = P("loop", "pair")
    return jax.shard_map(local, mesh=mesh, in_specs=in_specs, out_specs=out_specs, check_vma=False)
```

```python
import jax
import jax.numpy as jnp
from jax import lax
from jax.sharding import PartitionSpec as P

X, ZH, CORE = 4, 2, 2


def moved(x, axis, target):
    count = lax.axis_size(axis)
    return lax.ppermute(x, axis, [(i, target(i)) for i in range(count)])


def local(amplitudes, integrals, pair_partner, virtual_swap):
    loop_count = lax.axis_size("loop")
    pair_count = lax.axis_size("pair")
    ab_local = integrals.shape[0] // loop_count
    ij_local = amplitudes.shape[0]
    j = lax.axis_index("loop")
    x, zh, c = j // (ZH * CORE), (j // CORE) % ZH, j % CORE
    partial = lax.dot_general(
        integrals,
        amplitudes,
        (((1,), (1,)), ((), ())),
        precision=lax.Precision.HIGHEST,
        preferred_element_type=jnp.float32,
    )
    part = partial.reshape(X, ZH, CORE, ab_local, ij_local)
    keep = lax.dynamic_index_in_dim(part, c, axis=2, keepdims=False)
    give = lax.dynamic_index_in_dim(part, 1 - c, axis=2, keepdims=False)
    s1 = keep + moved(give, "loop", lambda i: i ^ 1)
    s2 = lax.dynamic_index_in_dim(s1, x, axis=0, keepdims=False)
    for shift in range(1, X):
        out = lax.dynamic_index_in_dim(s1, (x + shift) % X, axis=0, keepdims=False)
        s2 = s2 + moved(out, "loop", lambda i, s=shift: (((i // 4) + s) % X) * 4 + i % 4)
    mine = lax.dynamic_index_in_dim(s2, zh, axis=0, keepdims=False)
    other = lax.dynamic_index_in_dim(s2, 1 - zh, axis=0, keepdims=False)
    half = pair_count // 2
    from_zh = moved(other, "loop", lambda i: i ^ 2)
    from_pair = moved(mine, "pair", lambda i: (i + half) % pair_count)
    from_diag = moved(
        other,
        ("pair", "loop"),
        lambda i: ((i // loop_count + half) % pair_count) * loop_count + ((i % loop_count) ^ 2),
    )
    ladder = mine + from_zh
    mirror = from_pair + from_diag
    swap_local = virtual_swap - j * ab_local
    partner_local = pair_partner % ij_local
    mirror = jnp.take(jnp.take(mirror, swap_local, axis=0), partner_local, axis=1)
    return ladder + mirror


def solution(mesh):
    in_specs = (P("pair", "loop"), P(None, "loop"), P("pair"), P("loop"))
    out_specs = P("loop", "pair")
    return jax.shard_map(local, mesh=mesh, in_specs=in_specs, out_specs=out_specs, check_vma=False)
```

```python
import jax
import jax.numpy as jnp
from jax import lax
from jax.sharding import PartitionSpec as P

X, ZH, CORE = 4, 2, 2


def moved(x, axis, target):
    count = lax.axis_size(axis)
    return lax.ppermute(x, axis, [(i, target(i)) for i in range(count)])


def local(amplitudes, integrals, pair_partner, virtual_swap):
    loop_count = lax.axis_size("loop")
    pair_count = lax.axis_size("pair")
    ab_local = integrals.shape[0] // loop_count
    ij_local = amplitudes.shape[0]
    j = lax.axis_index("loop")
    x, zh, c = j // (ZH * CORE), (j // CORE) % ZH, j % CORE
    partial = lax.dot_general(
        integrals,
        amplitudes,
        (((1,), (1,)), ((), ())),
        precision=lax.Precision.HIGHEST,
        preferred_element_type=jnp.float32,
    )
    part = partial.reshape(X, ZH, CORE, ab_local, ij_local)
    keep = lax.dynamic_index_in_dim(part, c, axis=2, keepdims=False)
    give = lax.dynamic_index_in_dim(part, 1 - c, axis=2, keepdims=False)
    s1 = keep + moved(give, "loop", lambda i: i ^ 1)
    s2 = lax.dynamic_index_in_dim(s1, x, axis=0, keepdims=False)
    for shift in range(1, X):
        out = lax.dynamic_index_in_dim(s1, (x + shift) % X, axis=0, keepdims=False)
        s2 = s2 + moved(out, "loop", lambda i, s=shift: (((i // 4) + s) % X) * 4 + i % 4)
    mine = lax.dynamic_index_in_dim(s2, zh, axis=0, keepdims=False)
    other = lax.dynamic_index_in_dim(s2, 1 - zh, axis=0, keepdims=False)
    half = pair_count // 2
    from_diag = moved(
        other,
        ("pair", "loop"),
        lambda i: ((i // loop_count + half) % pair_count) * loop_count + ((i % loop_count) ^ 2),
    )
    swap_local = virtual_swap - j * ab_local
    partner_local = pair_partner % ij_local
    inverse = jnp.zeros((ij_local,), jnp.int32).at[partner_local].set(jnp.arange(ij_local, dtype=jnp.int32))
    to_pair = jnp.take(jnp.take(mine, swap_local, axis=0), inverse, axis=1) + from_diag
    from_pair = moved(to_pair, "pair", lambda i: (i + half) % pair_count)
    ladder = mine + from_pair
    mirror = jnp.take(jnp.take(from_diag, swap_local, axis=0), partner_local, axis=1)
    return ladder + mirror


def solution(mesh):
    in_specs = (P("pair", "loop"), P(None, "loop"), P("pair"), P("loop"))
    out_specs = P("loop", "pair")
    return jax.shard_map(local, mesh=mesh, in_specs=in_specs, out_specs=out_specs, check_vma=False)
```

```python
import jax
import jax.numpy as jnp
from jax import lax
from jax.sharding import Mesh, PartitionSpec as P

X, ZH, CORE = 4, 2, 2
PAIR = ("zl_hi", "zl_lo", "y")
LOOP = ("x", "zh", "core")


def moved(x, axis, target):
    count = lax.axis_size(axis)
    return lax.ppermute(x, axis, [(i, target(i)) for i in range(count)])


def local(amplitudes, integrals, pair_partner, virtual_swap):
    loop_count = lax.axis_size(LOOP)
    pair_count = lax.axis_size(PAIR)
    ab_local = integrals.shape[0] // loop_count
    ij_local = amplitudes.shape[0]
    j = lax.axis_index(LOOP)
    x, zh, c = j // (ZH * CORE), (j // CORE) % ZH, j % CORE
    partial = lax.dot_general(
        integrals,
        amplitudes,
        (((1,), (1,)), ((), ())),
        precision=lax.Precision.HIGHEST,
        preferred_element_type=jnp.float32,
    )
    part = partial.reshape(X, ZH, CORE, ab_local, ij_local)
    keep = lax.dynamic_index_in_dim(part, c, axis=2, keepdims=False)
    give = lax.dynamic_index_in_dim(part, 1 - c, axis=2, keepdims=False)
    s1 = keep + moved(give, LOOP, lambda i: i ^ 1)
    s2 = lax.all_to_all(s1, "x", 0, 0, tiled=True).reshape(X, ZH, ab_local, ij_local).sum(axis=0)
    mine = lax.dynamic_index_in_dim(s2, zh, axis=0, keepdims=False)
    other = lax.dynamic_index_in_dim(s2, 1 - zh, axis=0, keepdims=False)
    half = pair_count // 2
    from_zh = moved(other, LOOP, lambda i: i ^ 2)
    from_pair = moved(mine, PAIR, lambda i: (i + half) % pair_count)
    from_diag = moved(
        other,
        PAIR + LOOP,
        lambda i: ((i // loop_count + half) % pair_count) * loop_count + ((i % loop_count) ^ 2),
    )
    ladder = mine + from_zh
    mirror = from_pair + from_diag
    swap_local = virtual_swap - j * ab_local
    partner_local = pair_partner % ij_local
    mirror = jnp.take(jnp.take(mirror, swap_local, axis=0), partner_local, axis=1)
    return ladder + mirror


def solution(mesh):
    pair, loop = mesh.devices.shape
    fine = Mesh(mesh.devices.reshape(2, pair // (2 * 4), 4, X, ZH, CORE), PAIR + LOOP)
    in_specs = (P(PAIR, LOOP), P(None, LOOP), P(PAIR), P(LOOP))
    out_specs = P(LOOP, PAIR)
    return jax.shard_map(local, mesh=fine, in_specs=in_specs, out_specs=out_specs, check_vma=False)
```

```python
import jax
import jax.numpy as jnp
from jax import lax
from jax.sharding import Mesh, PartitionSpec as P

X, ZH, CORE = 4, 2, 2
PAIR = ("zl_hi", "zl_lo", "y")
LOOP = ("x", "zh", "core")


def moved(x, axis, target):
    count = lax.axis_size(axis)
    return lax.ppermute(x, axis, [(i, target(i)) for i in range(count)])


def local(amplitudes, integrals, pair_partner, virtual_swap):
    loop_count = lax.axis_size(LOOP)
    pair_count = lax.axis_size(PAIR)
    ab_local = integrals.shape[0] // loop_count
    ij_local = amplitudes.shape[0]
    j = lax.axis_index(LOOP)
    x, zh, c = j // (ZH * CORE), (j // CORE) % ZH, j % CORE
    partial = lax.dot_general(
        integrals,
        amplitudes,
        (((1,), (1,)), ((), ())),
        precision=lax.Precision.HIGHEST,
        preferred_element_type=jnp.float32,
    )
    part = partial.reshape(X, ZH, CORE, ab_local, ij_local)
    keep = lax.dynamic_index_in_dim(part, c, axis=2, keepdims=False)
    give = lax.dynamic_index_in_dim(part, 1 - c, axis=2, keepdims=False)
    s1 = keep + moved(give, LOOP, lambda i: i ^ 1)
    s2 = lax.all_to_all(s1, "x", 0, 0, tiled=True).reshape(X, ZH, ab_local, ij_local).sum(axis=0)
    zl = lax.axis_index("zl_hi")
    sent = jnp.broadcast_to(s2[None], (2,) + s2.shape).reshape(2 * ZH, ab_local, ij_local)
    got = lax.all_to_all(sent, ("zl_hi", "zh"), 0, 0, tiled=True).reshape(2, ZH, ab_local, ij_local).sum(axis=1)
    ladder = lax.dynamic_index_in_dim(got, zl, axis=0, keepdims=False)
    mirror = lax.dynamic_index_in_dim(got, 1 - zl, axis=0, keepdims=False)
    swap_local = virtual_swap - j * ab_local
    partner_local = pair_partner % ij_local
    mirror = jnp.take(jnp.take(mirror, swap_local, axis=0), partner_local, axis=1)
    return ladder + mirror


def solution(mesh):
    pair, loop = mesh.devices.shape
    fine = Mesh(mesh.devices.reshape(2, pair // (2 * 4), 4, X, ZH, CORE), PAIR + LOOP)
    in_specs = (P(PAIR, LOOP), P(None, LOOP), P(PAIR), P(LOOP))
    out_specs = P(LOOP, PAIR)
    return jax.shard_map(local, mesh=fine, in_specs=in_specs, out_specs=out_specs, check_vma=False)
```

```python
import jax
import jax.numpy as jnp
from jax import lax
from jax.sharding import Mesh, PartitionSpec as P

X, ZH, CORE = 4, 2, 2
PAIR = ("zl_hi", "zl_lo", "y")
LOOP = ("x", "zh", "core")
CHUNK = 64


def moved(x, axis, target):
    count = lax.axis_size(axis)
    return lax.ppermute(x, axis, [(i, target(i)) for i in range(count)])


def local(amplitudes, integrals, pair_partner, virtual_swap):
    loop_count = lax.axis_size(LOOP)
    pair_count = lax.axis_size(PAIR)
    ab_local = integrals.shape[0] // loop_count
    ij_local = amplitudes.shape[0]
    chunks = ab_local // CHUNK
    j = lax.axis_index(LOOP)
    x, zh, c = j // (ZH * CORE), (j // CORE) % ZH, j % CORE
    half = pair_count // 2
    swap_local = virtual_swap - j * ab_local
    partner_local = pair_partner % ij_local
    rows = integrals.reshape(loop_count, chunks, CHUNK, integrals.shape[1])
    outs = []
    for h in range(chunks):
        partial = lax.dot_general(
            rows[:, h].reshape(loop_count * CHUNK, integrals.shape[1]),
            amplitudes,
            (((1,), (1,)), ((), ())),
            precision=lax.Precision.HIGHEST,
            preferred_element_type=jnp.float32,
        )
        part = partial.reshape(X, ZH, CORE, CHUNK, ij_local)
        keep = lax.dynamic_index_in_dim(part, c, axis=2, keepdims=False)
        give = lax.dynamic_index_in_dim(part, 1 - c, axis=2, keepdims=False)
        s1 = keep + moved(give, LOOP, lambda i: i ^ 1)
        s2 = lax.all_to_all(s1, "x", 0, 0, tiled=True).reshape(X, ZH, CHUNK, ij_local).sum(axis=0)
        mine = lax.dynamic_index_in_dim(s2, zh, axis=0, keepdims=False)
        other = lax.dynamic_index_in_dim(s2, 1 - zh, axis=0, keepdims=False)
        from_zh = moved(other, LOOP, lambda i: i ^ 2)
        from_pair = moved(mine, PAIR, lambda i: (i + half) % pair_count)
        from_diag = moved(
            other,
            PAIR + LOOP,
            lambda i: ((i // loop_count + half) % pair_count) * loop_count + ((i % loop_count) ^ 2),
        )
        ladder = mine + from_zh
        mirror = from_pair + from_diag
        swap_chunk = swap_local[h * CHUNK:(h + 1) * CHUNK] - h * CHUNK
        mirror = jnp.take(jnp.take(mirror, swap_chunk, axis=0), partner_local, axis=1)
        outs.append(ladder + mirror)
    return jnp.concatenate(outs, axis=0)


def solution(mesh):
    pair, loop = mesh.devices.shape
    fine = Mesh(mesh.devices.reshape(2, pair // (2 * 4), 4, X, ZH, CORE), PAIR + LOOP)
    in_specs = (P(PAIR, LOOP), P(None, LOOP), P(PAIR), P(LOOP))
    out_specs = P(LOOP, PAIR)
    return jax.shard_map(local, mesh=fine, in_specs=in_specs, out_specs=out_specs, check_vma=False)
```

```python
import jax
import jax.numpy as jnp
from jax import lax
from jax.sharding import Mesh, PartitionSpec as P

X, ZH, CORE = 4, 2, 2
PAIR = ("zl_hi", "zl_lo", "y")
LOOP = ("x", "zh", "core")


def moved(x, axis, target):
    count = lax.axis_size(axis)
    return lax.ppermute(x, axis, [(i, target(i)) for i in range(count)])


def local(amplitudes, integrals, pair_partner, virtual_swap):
    loop_count = lax.axis_size(LOOP)
    pair_count = lax.axis_size(PAIR)
    ab_local = integrals.shape[0] // loop_count
    ij_local = amplitudes.shape[0]
    j = lax.axis_index(LOOP)
    x, zh, c = j // (ZH * CORE), (j // CORE) % ZH, j % CORE
    blocks = integrals.reshape(X, ZH, CORE, ab_local, integrals.shape[1])

    def product(core):
        rows = lax.dynamic_index_in_dim(blocks, core, axis=2, keepdims=False)
        return lax.dot_general(
            rows.reshape(X * ZH * ab_local, integrals.shape[1]),
            amplitudes,
            (((1,), (1,)), ((), ())),
            precision=lax.Precision.HIGHEST,
            preferred_element_type=jnp.float32,
        ).reshape(X, ZH, ab_local, ij_local)

    give = moved(product(1 - c), LOOP, lambda i: i ^ 1)
    s1 = lax.optimization_barrier(product(c)) + give
    s2 = lax.all_to_all(s1, "x", 0, 0, tiled=True).reshape(X, ZH, ab_local, ij_local).sum(axis=0)
    mine = lax.dynamic_index_in_dim(s2, zh, axis=0, keepdims=False)
    other = lax.dynamic_index_in_dim(s2, 1 - zh, axis=0, keepdims=False)
    half = pair_count // 2
    from_zh = moved(other, LOOP, lambda i: i ^ 2)
    from_pair = moved(mine, PAIR, lambda i: (i + half) % pair_count)
    from_diag = moved(
        other,
        PAIR + LOOP,
        lambda i: ((i // loop_count + half) % pair_count) * loop_count + ((i % loop_count) ^ 2),
    )
    ladder = mine + from_zh
    mirror = from_pair + from_diag
    swap_local = virtual_swap - j * ab_local
    partner_local = pair_partner % ij_local
    mirror = jnp.take(jnp.take(mirror, swap_local, axis=0), partner_local, axis=1)
    return ladder + mirror


def solution(mesh):
    pair, loop = mesh.devices.shape
    fine = Mesh(mesh.devices.reshape(2, pair // (2 * 4), 4, X, ZH, CORE), PAIR + LOOP)
    in_specs = (P(PAIR, LOOP), P(None, LOOP), P(PAIR), P(LOOP))
    out_specs = P(LOOP, PAIR)
    return jax.shard_map(local, mesh=fine, in_specs=in_specs, out_specs=out_specs, check_vma=False)
```

```python
import jax
import jax.numpy as jnp
from jax import lax
from jax.sharding import Mesh, PartitionSpec as P

X, ZH, CORE = 4, 2, 2
PAIR = ("zl_hi", "zl_lo", "y")
LOOP = ("x", "zh", "core")


def moved(x, axis, target):
    count = lax.axis_size(axis)
    return lax.ppermute(x, axis, [(i, target(i)) for i in range(count)])


def local(amplitudes, integrals, pair_partner, virtual_swap):
    loop_count = lax.axis_size(LOOP)
    pair_count = lax.axis_size(PAIR)
    ab_local = integrals.shape[0] // loop_count
    ij_local = amplitudes.shape[0]
    j = lax.axis_index(LOOP)
    x, zh, c = j // (ZH * CORE), (j // CORE) % ZH, j % CORE
    blocks = integrals.reshape(X, ZH, CORE, ab_local, integrals.shape[1])

    def product(core):
        rows = lax.dynamic_index_in_dim(blocks, core, axis=2, keepdims=False)
        return lax.dot_general(
            rows.reshape(X * ZH * ab_local, integrals.shape[1]),
            amplitudes,
            (((1,), (1,)), ((), ())),
            precision=lax.Precision.HIGHEST,
            preferred_element_type=jnp.float32,
        ).reshape(X, ZH, ab_local, ij_local)

    give = moved(product(1 - c), LOOP, lambda i: i ^ 1)
    s1 = lax.optimization_barrier(product(c)) + give
    s2 = lax.all_to_all(s1, "x", 0, 0, tiled=True).reshape(X, ZH, ab_local, ij_local).sum(axis=0)
    mine = lax.dynamic_index_in_dim(s2, zh, axis=0, keepdims=False)
    other = lax.dynamic_index_in_dim(s2, 1 - zh, axis=0, keepdims=False)
    half = pair_count // 2
    from_diag = moved(
        other,
        PAIR + LOOP,
        lambda i: ((i // loop_count + half) % pair_count) * loop_count + ((i % loop_count) ^ 2),
    )
    swap_local = virtual_swap - j * ab_local
    partner_local = pair_partner % ij_local
    inverse = jnp.zeros((ij_local,), jnp.int32).at[partner_local].set(jnp.arange(ij_local, dtype=jnp.int32))
    to_pair = jnp.take(jnp.take(mine, swap_local, axis=0), inverse, axis=1) + from_diag
    from_pair = moved(to_pair, PAIR, lambda i: (i + half) % pair_count)
    ladder = mine + from_pair
    mirror = jnp.take(jnp.take(from_diag, swap_local, axis=0), partner_local, axis=1)
    return ladder + mirror


def solution(mesh):
    pair, loop = mesh.devices.shape
    fine = Mesh(mesh.devices.reshape(2, pair // (2 * 4), 4, X, ZH, CORE), PAIR + LOOP)
    in_specs = (P(PAIR, LOOP), P(None, LOOP), P(PAIR), P(LOOP))
    out_specs = P(LOOP, PAIR)
    return jax.shard_map(local, mesh=fine, in_specs=in_specs, out_specs=out_specs, check_vma=False)
```

```python
import jax
import jax.numpy as jnp
from jax import lax
from jax.sharding import Mesh, PartitionSpec as P


X, ZH, CORE = 4, 2, 2
PAIR = ("zl_hi", "zl_lo", "y")
LOOP = ("x", "zh", "core")


def moved(x, axis, target):
    count = lax.axis_size(axis)
    return lax.ppermute(x, axis, [(i, target(i)) for i in range(count)])


def body(amplitudes, integrals, pair_partner, virtual_swap):
    loop_count = lax.axis_size(LOOP)
    pair_count = lax.axis_size(PAIR)
    ab_local = integrals.shape[0] // loop_count
    ij_local = amplitudes.shape[0]
    j = lax.axis_index(LOOP)
    zh, c = (j // CORE) % ZH, j % CORE
    blocks = integrals.reshape(X, ZH, CORE, ab_local, integrals.shape[1])

    def product(core):
        rows = lax.dynamic_index_in_dim(blocks, core, axis=2, keepdims=False)
        return lax.dot_general(
            rows.reshape(X * ZH * ab_local, integrals.shape[1]),
            amplitudes,
            (((1,), (1,)), ((), ())),
            precision=lax.Precision.HIGHEST,
            preferred_element_type=jnp.float32,
        ).reshape(X, ZH, ab_local, ij_local)

    give = moved(product(1 - c), LOOP, lambda i: i ^ 1)
    s1 = lax.optimization_barrier(product(c)) + give
    s2 = lax.all_to_all(s1, "x", 0, 0, tiled=True).reshape(X, ZH, ab_local, ij_local).sum(axis=0)
    mine = lax.dynamic_index_in_dim(s2, zh, axis=0, keepdims=False)
    other = lax.dynamic_index_in_dim(s2, 1 - zh, axis=0, keepdims=False)
    half = pair_count // 2
    from_zh = moved(other, LOOP, lambda i: i ^ 2)
    from_pair = moved(mine, PAIR, lambda i: (i + half) % pair_count)
    from_diag = moved(
        other,
        PAIR + LOOP,
        lambda i: ((i // loop_count + half) % pair_count) * loop_count + ((i % loop_count) ^ 2),
    )
    ladder = mine + from_zh
    mirror = from_pair + from_diag
    swap_local = virtual_swap - j * ab_local
    partner_local = pair_partner % ij_local
    mirror = jnp.take(jnp.take(mirror, swap_local, axis=0), partner_local, axis=1)
    return ladder + mirror


def solution(mesh):
    pair, _ = mesh.devices.shape
    fine = Mesh(mesh.devices.reshape(2, pair // (2 * 4), 4, X, ZH, CORE), PAIR + LOOP)
    in_specs = (P(PAIR, LOOP), P(None, LOOP), P(PAIR), P(LOOP))
    out_specs = P(LOOP, PAIR)
    return jax.shard_map(body, mesh=fine, in_specs=in_specs, out_specs=out_specs, check_vma=False)
```

```python
import jax
import jax.numpy as jnp
from jax import lax
from jax.sharding import Mesh, PartitionSpec as P

X, ZH, CORE = 4, 2, 2
PAIR = ("zl_hi", "zl_lo", "y")
LOOP = ("x", "zh", "core")


def moved(x, axis, target):
    count = lax.axis_size(axis)
    return lax.ppermute(x, axis, [(i, target(i)) for i in range(count)])


def local(amplitudes, integrals, pair_partner, virtual_swap):
    loop_count = lax.axis_size(LOOP)
    pair_count = lax.axis_size(PAIR)
    ab_local = integrals.shape[0] // loop_count
    ij_local = amplitudes.shape[0]
    j = lax.axis_index(LOOP)
    x, zh, c = j // (ZH * CORE), (j // CORE) % ZH, j % CORE
    blocks = integrals.reshape(X, ZH, CORE, ab_local, integrals.shape[1])

    def product(core):
        rows = lax.dynamic_index_in_dim(blocks, core, axis=2, keepdims=False)
        return lax.dot_general(
            rows.reshape(X * ZH * ab_local, integrals.shape[1]),
            amplitudes,
            (((1,), (1,)), ((), ())),
            precision=lax.Precision.HIGH,
            preferred_element_type=jnp.float32,
        ).reshape(X, ZH, ab_local, ij_local)

    give = moved(product(1 - c), LOOP, lambda i: i ^ 1)
    s1 = lax.optimization_barrier(product(c)) + give
    s2 = lax.all_to_all(s1, "x", 0, 0, tiled=True).reshape(X, ZH, ab_local, ij_local).sum(axis=0)
    mine = lax.dynamic_index_in_dim(s2, zh, axis=0, keepdims=False)
    other = lax.dynamic_index_in_dim(s2, 1 - zh, axis=0, keepdims=False)
    half = pair_count // 2
    from_zh = moved(other, LOOP, lambda i: i ^ 2)
    from_pair = moved(mine, PAIR, lambda i: (i + half) % pair_count)
    from_diag = moved(
        other,
        PAIR + LOOP,
        lambda i: ((i // loop_count + half) % pair_count) * loop_count + ((i % loop_count) ^ 2),
    )
    ladder = mine + from_zh
    mirror = from_pair + from_diag
    swap_local = virtual_swap - j * ab_local
    partner_local = pair_partner % ij_local
    mirror = jnp.take(jnp.take(mirror, swap_local, axis=0), partner_local, axis=1)
    return ladder + mirror


def solution(mesh):
    pair, loop = mesh.devices.shape
    fine = Mesh(mesh.devices.reshape(2, pair // (2 * 4), 4, X, ZH, CORE), PAIR + LOOP)
    in_specs = (P(PAIR, LOOP), P(None, LOOP), P(PAIR), P(LOOP))
    out_specs = P(LOOP, PAIR)
    return jax.shard_map(local, mesh=fine, in_specs=in_specs, out_specs=out_specs, check_vma=False)
```

```python
import jax
import jax.numpy as jnp
from jax import lax
from jax.sharding import Mesh, PartitionSpec as P


X, ZH, CORE = 4, 2, 2
PAIR = ("zl_hi", "zl_lo", "y")
LOOP = ("x", "zh", "core")


def moved(x, axis, target):
    count = lax.axis_size(axis)
    return lax.ppermute(x, axis, [(i, target(i)) for i in range(count)])


def body(amplitudes, integrals, pair_partner, virtual_swap):
    loop_count = lax.axis_size(LOOP)
    pair_count = lax.axis_size(PAIR)
    ab_local = integrals.shape[0] // loop_count
    ij_local = amplitudes.shape[0]
    j = lax.axis_index(LOOP)
    zh, c = (j // CORE) % ZH, j % CORE
    blocks = integrals.reshape(X, ZH, CORE, ab_local, integrals.shape[1])

    def product(core):
        rows = lax.dynamic_index_in_dim(blocks, core, axis=2, keepdims=False)
        return lax.dot_general(
            rows.reshape(X * ZH * ab_local, integrals.shape[1]),
            amplitudes,
            (((1,), (1,)), ((), ())),
            precision=lax.Precision.HIGHEST,
            preferred_element_type=jnp.float32,
        ).reshape(X, ZH, ab_local, ij_local)

    give = moved(product(1 - c), LOOP, lambda i: i ^ 1)
    s1 = lax.optimization_barrier(product(c)) + give

    def along_x(rows):
        return lax.all_to_all(rows, "x", 0, 0, tiled=True).reshape(X, ab_local, ij_local).sum(axis=0)

    other = along_x(lax.dynamic_index_in_dim(s1, 1 - zh, axis=1, keepdims=False))
    half = pair_count // 2
    from_zh = moved(other, LOOP, lambda i: i ^ 2)
    from_diag = moved(
        other,
        PAIR + LOOP,
        lambda i: ((i // loop_count + half) % pair_count) * loop_count + ((i % loop_count) ^ 2),
    )
    mine = along_x(lax.dynamic_index_in_dim(s1, zh, axis=1, keepdims=False))
    from_pair = moved(mine, PAIR, lambda i: (i + half) % pair_count)
    ladder = mine + from_zh
    mirror = from_pair + from_diag
    swap_local = virtual_swap - j * ab_local
    partner_local = pair_partner % ij_local
    mirror = jnp.take(jnp.take(mirror, swap_local, axis=0), partner_local, axis=1)
    return ladder + mirror


def solution(mesh):
    pair, _ = mesh.devices.shape
    fine = Mesh(mesh.devices.reshape(2, pair // (2 * 4), 4, X, ZH, CORE), PAIR + LOOP)
    in_specs = (P(PAIR, LOOP), P(None, LOOP), P(PAIR), P(LOOP))
    out_specs = P(LOOP, PAIR)
    return jax.shard_map(body, mesh=fine, in_specs=in_specs, out_specs=out_specs, check_vma=False)
```

```python
import jax
import jax.numpy as jnp
from jax import lax
from jax.sharding import Mesh, PartitionSpec as P

X, ZH, CORE = 4, 2, 2
PAIR = ("zl_hi", "zl_lo", "y")
LOOP = ("x", "zh", "core")


def moved(x, axis, target):
    count = lax.axis_size(axis)
    return lax.ppermute(x, axis, [(i, target(i)) for i in range(count)])


def local(amplitudes, integrals, pair_partner, virtual_swap):
    loop_count = lax.axis_size(LOOP)
    pair_count = lax.axis_size(PAIR)
    ab_local = integrals.shape[0] // loop_count
    ij_local = amplitudes.shape[0]
    j = lax.axis_index(LOOP)
    x, zh, c = j // (ZH * CORE), (j // CORE) % ZH, j % CORE
    blocks = integrals.reshape(X, ZH, CORE, ab_local, integrals.shape[1])

    def product(core, precision):
        rows = lax.dynamic_index_in_dim(blocks, core, axis=2, keepdims=False)
        return lax.dot_general(
            rows.reshape(X * ZH * ab_local, integrals.shape[1]),
            amplitudes,
            (((1,), (1,)), ((), ())),
            precision=precision,
            preferred_element_type=jnp.float32,
        ).reshape(X, ZH, ab_local, ij_local)

    give = moved(product(1 - c, lax.Precision.HIGH), LOOP, lambda i: i ^ 1)
    s1 = lax.optimization_barrier(product(c, lax.Precision.HIGHEST)) + give
    s2 = lax.all_to_all(s1, "x", 0, 0, tiled=True).reshape(X, ZH, ab_local, ij_local).sum(axis=0)
    mine = lax.dynamic_index_in_dim(s2, zh, axis=0, keepdims=False)
    other = lax.dynamic_index_in_dim(s2, 1 - zh, axis=0, keepdims=False)
    half = pair_count // 2
    from_zh = moved(other, LOOP, lambda i: i ^ 2)
    from_pair = moved(mine, PAIR, lambda i: (i + half) % pair_count)
    from_diag = moved(
        other,
        PAIR + LOOP,
        lambda i: ((i // loop_count + half) % pair_count) * loop_count + ((i % loop_count) ^ 2),
    )
    ladder = mine + from_zh
    mirror = from_pair + from_diag
    swap_local = virtual_swap - j * ab_local
    partner_local = pair_partner % ij_local
    mirror = jnp.take(jnp.take(mirror, swap_local, axis=0), partner_local, axis=1)
    return ladder + mirror


def solution(mesh):
    pair, loop = mesh.devices.shape
    fine = Mesh(mesh.devices.reshape(2, pair // (2 * 4), 4, X, ZH, CORE), PAIR + LOOP)
    in_specs = (P(PAIR, LOOP), P(None, LOOP), P(PAIR), P(LOOP))
    out_specs = P(LOOP, PAIR)
    return jax.shard_map(local, mesh=fine, in_specs=in_specs, out_specs=out_specs, check_vma=False)
```

```python
import jax
import jax.numpy as jnp
from jax import lax
from jax.sharding import Mesh, PartitionSpec as P

X, ZH, CORE = 4, 2, 2
PAIR = ("zl_hi", "zl_lo", "y")
LOOP = ("x", "zh", "core")


def moved(x, axis, target):
    count = lax.axis_size(axis)
    return lax.ppermute(x, axis, [(i, target(i)) for i in range(count)])


def local(amplitudes, integrals, pair_partner, virtual_swap):
    loop_count = lax.axis_size(LOOP)
    pair_count = lax.axis_size(PAIR)
    ab_local = integrals.shape[0] // loop_count
    ij_local = amplitudes.shape[0]
    j = lax.axis_index(LOOP)
    x, zh, c = j // (ZH * CORE), (j // CORE) % ZH, j % CORE
    blocks = integrals.reshape(X, ZH, CORE, ab_local, integrals.shape[1])

    def product(core):
        rows = lax.dynamic_index_in_dim(blocks, core, axis=2, keepdims=False)
        return lax.dot_general(
            rows.reshape(X * ZH * ab_local, integrals.shape[1]),
            amplitudes,
            (((1,), (1,)), ((), ())),
            precision=lax.Precision.HIGHEST,
            preferred_element_type=jnp.float32,
        ).reshape(X, ZH, ab_local, ij_local)

    give = moved(product(1 - c), LOOP, lambda i: i ^ 1)
    s1 = lax.optimization_barrier(product(c)) + give
    s2 = lax.all_to_all(s1, "x", 0, 0, tiled=True).reshape(X, ZH, ab_local, ij_local).sum(axis=0)
    mine = lax.dynamic_index_in_dim(s2, zh, axis=0, keepdims=False)
    other = lax.dynamic_index_in_dim(s2, 1 - zh, axis=0, keepdims=False)
    half = pair_count // 2
    from_zh = lax.dynamic_index_in_dim(lax.all_to_all(s2, "zh", 0, 0, tiled=True), 1 - zh, axis=0, keepdims=False)
    from_pair = moved(mine, PAIR, lambda i: (i + half) % pair_count)
    from_diag = moved(
        other,
        PAIR + LOOP,
        lambda i: ((i // loop_count + half) % pair_count) * loop_count + ((i % loop_count) ^ 2),
    )
    ladder = mine + from_zh
    mirror = from_pair + from_diag
    swap_local = virtual_swap - j * ab_local
    partner_local = pair_partner % ij_local
    mirror = jnp.take(jnp.take(mirror, swap_local, axis=0), partner_local, axis=1)
    return ladder + mirror


def solution(mesh):
    pair, loop = mesh.devices.shape
    fine = Mesh(mesh.devices.reshape(2, pair // (2 * 4), 4, X, ZH, CORE), PAIR + LOOP)
    in_specs = (P(PAIR, LOOP), P(None, LOOP), P(PAIR), P(LOOP))
    out_specs = P(LOOP, PAIR)
    return jax.shard_map(local, mesh=fine, in_specs=in_specs, out_specs=out_specs, check_vma=False)
```

```python
import jax
import jax.numpy as jnp
from jax import lax
from jax.sharding import Mesh, PartitionSpec as P

X, ZH, CORE = 4, 2, 2
PAIR = ("zl_hi", "zl_lo", "y")
LOOP = ("x", "zh", "core")


def moved(x, axis, target):
    count = lax.axis_size(axis)
    return lax.ppermute(x, axis, [(i, target(i)) for i in range(count)])


def local(amplitudes, integrals, pair_partner, virtual_swap):
    loop_count = lax.axis_size(LOOP)
    pair_count = lax.axis_size(PAIR)
    ab_local = integrals.shape[0] // loop_count
    ij_local = amplitudes.shape[0]
    j = lax.axis_index(LOOP)
    x, zh, c = j // (ZH * CORE), (j // CORE) % ZH, j % CORE
    blocks = integrals.reshape(X, ZH, CORE, ab_local, integrals.shape[1])

    def product(core):
        rows = lax.dynamic_index_in_dim(blocks, core, axis=2, keepdims=False)
        return lax.dot_general(
            rows.reshape(X * ZH * ab_local, integrals.shape[1]),
            amplitudes,
            (((1,), (1,)), ((), ())),
            precision=lax.Precision.HIGHEST,
            preferred_element_type=jnp.float32,
        ).reshape(X, ZH, ab_local, ij_local)

    give = moved(product(1 - c), LOOP, lambda i: i ^ 1)
    s1 = lax.optimization_barrier(product(c)) + give
    s2 = lax.dynamic_index_in_dim(s1, x, axis=0, keepdims=False)
    for shift in (2, 1, 3):
        out = lax.dynamic_index_in_dim(s1, (x + shift) % X, axis=0, keepdims=False)
        s2 = s2 + moved(out, LOOP, lambda i, s=shift: (((i // 4) + s) % X) * 4 + i % 4)
    mine = lax.dynamic_index_in_dim(s2, zh, axis=0, keepdims=False)
    other = lax.dynamic_index_in_dim(s2, 1 - zh, axis=0, keepdims=False)
    half = pair_count // 2
    from_zh = moved(other, LOOP, lambda i: i ^ 2)
    from_pair = moved(mine, PAIR, lambda i: (i + half) % pair_count)
    from_diag = moved(
        other,
        PAIR + LOOP,
        lambda i: ((i // loop_count + half) % pair_count) * loop_count + ((i % loop_count) ^ 2),
    )
    ladder = mine + from_zh
    mirror = from_pair + from_diag
    swap_local = virtual_swap - j * ab_local
    partner_local = pair_partner % ij_local
    mirror = jnp.take(jnp.take(mirror, swap_local, axis=0), partner_local, axis=1)
    return ladder + mirror


def solution(mesh):
    pair, loop = mesh.devices.shape
    fine = Mesh(mesh.devices.reshape(2, pair // (2 * 4), 4, X, ZH, CORE), PAIR + LOOP)
    in_specs = (P(PAIR, LOOP), P(None, LOOP), P(PAIR), P(LOOP))
    out_specs = P(LOOP, PAIR)
    return jax.shard_map(local, mesh=fine, in_specs=in_specs, out_specs=out_specs, check_vma=False)
```

```python
import jax
import jax.numpy as jnp
from jax import lax
from jax.sharding import Mesh, PartitionSpec as P

X, ZH, CORE = 4, 2, 2
PAIR = ("zl_hi", "zl_lo", "y")
LOOP = ("x", "zh", "core")


def moved(x, axis, target):
    count = lax.axis_size(axis)
    return lax.ppermute(x, axis, [(i, target(i)) for i in range(count)])


def local(amplitudes, integrals, pair_partner, virtual_swap):
    loop_count = lax.axis_size(LOOP)
    pair_count = lax.axis_size(PAIR)
    ab_local = integrals.shape[0] // loop_count
    ij_local = amplitudes.shape[0]
    j = lax.axis_index(LOOP)
    x, zh, c = j // (ZH * CORE), (j // CORE) % ZH, j % CORE
    blocks = integrals.reshape(X, ZH, CORE, ab_local, integrals.shape[1])

    def product(core):
        rows = lax.dynamic_index_in_dim(blocks, core, axis=2, keepdims=False)
        return lax.dot_general(
            rows.reshape(X * ZH * ab_local, integrals.shape[1]),
            amplitudes,
            (((1,), (1,)), ((), ())),
            precision=lax.Precision.HIGHEST,
            preferred_element_type=jnp.float32,
        ).reshape(X, ZH, ab_local, ij_local)

    give = moved(product(1 - c), LOOP, lambda i: i ^ 1)
    s1 = lax.optimization_barrier(product(c)) + give
    s2 = lax.dynamic_index_in_dim(s1, x, axis=0, keepdims=False)
    for shift in (2, 3, 1):
        out = lax.dynamic_index_in_dim(s1, (x + shift) % X, axis=0, keepdims=False)
        s2 = s2 + moved(out, LOOP, lambda i, s=shift: (((i // 4) + s) % X) * 4 + i % 4)
    mine = lax.dynamic_index_in_dim(s2, zh, axis=0, keepdims=False)
    other = lax.dynamic_index_in_dim(s2, 1 - zh, axis=0, keepdims=False)
    half = pair_count // 2
    from_zh = moved(other, LOOP, lambda i: i ^ 2)
    from_pair = moved(mine, PAIR, lambda i: (i + half) % pair_count)
    from_diag = moved(
        other,
        PAIR + LOOP,
        lambda i: ((i // loop_count + half) % pair_count) * loop_count + ((i % loop_count) ^ 2),
    )
    ladder = mine + from_zh
    mirror = from_pair + from_diag
    swap_local = virtual_swap - j * ab_local
    partner_local = pair_partner % ij_local
    mirror = jnp.take(jnp.take(mirror, swap_local, axis=0), partner_local, axis=1)
    return ladder + mirror


def solution(mesh):
    pair, loop = mesh.devices.shape
    fine = Mesh(mesh.devices.reshape(2, pair // (2 * 4), 4, X, ZH, CORE), PAIR + LOOP)
    in_specs = (P(PAIR, LOOP), P(None, LOOP), P(PAIR), P(LOOP))
    out_specs = P(LOOP, PAIR)
    return jax.shard_map(local, mesh=fine, in_specs=in_specs, out_specs=out_specs, check_vma=False)
```
